512 devices in a mesh: leaf: 32 (over z, core), sub: 16 (over x, y).
Axes of the slice: x: 4, y: 4, z: 16, core: 2. Of those that a mesh axis runs over, the one named last changes fastest.
Arguments:
- right_side: float32 [2048, 32, 256], P(('leaf', 'sub'))
- points: float32 [2048, 3, 256], P(('leaf', 'sub')), may hold values from 0 to 32, as said below
- near_boxes: int32 [2048, 27], P(('leaf', 'sub')), may hold values from -1 to 2047, as said below
Outputs:
- solution_field: float32 [2048, 32, 256], P(('leaf', 'sub'))
- residual: float32 [2048, 32, 256], P(('leaf', 'sub'))
The draws below stay inside these ranges and needn't reach their ends.
Inputs may be any that keep to these rules, and one draw needn't show every extreme that they name: `near_boxes`: each box's points lie in one unit cube with integer corner. A box lists itself and exactly the boxes whose cubes touch its own (faces, edges or corners), and -1 in its other entries. Every listed box lies on a device whose grid position differs by at most one in each of the three grid dimensions, where a device's index over leaf+sub is gx * 4 * 8 + gy * 8 + gz. Each box's points lie in its unit cube, the cubes of one device forming a block of 2 x 2 x 1.
All inputs are finite; a program needn't handle non-finite values.
Results may differ from the reference program's by a relative error of at most 0.0003.
Values sent between devices are 32-bit elements; how exact they have to be, the bound alone decides.
No kernel may reach another device: no remote copies, remote signals or barrier semaphores. Data moves between devices by JAX's collectives and lax.ppermute only.
A program may use at most 64 MiB of HBM per device.

```python
import jax
import jax.numpy as jnp
from jax import lax

DEPTH = 1
PTS = 256
RHS = 32
ITERS = 2
GRID_Y = 4
BOX_DEV = 4
GRID_X = 16
GRID_Z = 8
BOXES = 2048


def layout_cells(key):
    groups = BOXES // BOX_DEV
    scores = jax.random.randint(jax.random.fold_in(key, 11), (groups, BOX_DEV), 0, 1 << 20)
    scores = scores * BOX_DEV + jnp.arange(BOX_DEV, dtype=jnp.int32)[None, :]
    cell_of_slot = jnp.argsort(scores, axis=1, stable=True).astype(jnp.int32)
    slot_of_cell = jnp.argsort(cell_of_slot, axis=1, stable=True).astype(jnp.int32)
    return (cell_of_slot, slot_of_cell)


def global_cells(cell_of_slot):
    cells = cell_of_slot.reshape(-1)
    owner_dev = jnp.arange(BOXES, dtype=jnp.int32) // BOX_DEV
    grid_xpos = owner_dev // (GRID_Y * GRID_Z)
    grid_ypos = owner_dev // GRID_Z % GRID_Y
    grid_zpos = owner_dev % GRID_Z
    cell_xpos = 2 * grid_xpos + cells // (2 * DEPTH)
    cell_ypos = 2 * grid_ypos + cells // DEPTH % 2
    cell_zpos = DEPTH * grid_zpos + cells % DEPTH
    return (cell_xpos, cell_ypos, cell_zpos)


def draw_near_boxes(key, part):
    layout = layout_cells(key)
    slot_of_cell = layout[1]
    cell_xpos, cell_ypos, cell_zpos = global_cells(layout[0])
    columns = []
    for step_x in (-1, 0, 1):
        for step_y in (-1, 0, 1):
            for step_z in (-1, 0, 1):
                moved_x = cell_xpos + step_x
                moved_y = cell_ypos + step_y
                moved_z = cell_zpos + step_z
                inside = (moved_x >= 0) & (moved_x < 2 * GRID_X) & (moved_y >= 0) & (moved_y < 2 * GRID_Y) & (moved_z >= 0) & (moved_z < DEPTH * GRID_Z)
                clamp_x = jnp.clip(moved_x, 0, 2 * GRID_X - 1)
                clamp_y = jnp.clip(moved_y, 0, 2 * GRID_Y - 1)
                clamp_z = jnp.clip(moved_z, 0, DEPTH * GRID_Z - 1)
                target_dev = clamp_x // 2 * GRID_Y * GRID_Z + clamp_y // 2 * GRID_Z + clamp_z // DEPTH
                target_cell = clamp_x % 2 * 2 * DEPTH + clamp_y % 2 * DEPTH + clamp_z % DEPTH
                target_slot = slot_of_cell[target_dev, target_cell]
                columns.append(jnp.where(inside, target_dev * BOX_DEV + target_slot, -1))
    return jnp.stack(columns, axis=1).astype(jnp.int32)


def draw_points(key, part):
    layout = layout_cells(key)
    corner = jnp.stack(global_cells(layout[0]), axis=1).astype(jnp.float32)
    offsets_in = jax.random.uniform(jax.random.fold_in(key, 5), (BOXES, 3, PTS), jnp.float32)
    return corner[:, :, None] + offsets_in


def draw_right_side(key, part):
    owner_dev = (jnp.arange(BOXES, dtype=jnp.int32) // BOX_DEV).astype(jnp.float32)
    devices_all = BOXES // BOX_DEV
    rising = 1.0 + 2.0 * owner_dev / max(devices_all - 1, 1)
    normals = jax.random.normal(jax.random.fold_in(key, 3), (BOXES, RHS, PTS), jnp.float32)
    return normals * rising[:, None, None]


def setup_inputs(seed: int = 0) -> dict:
    splits = jax.random.split(jax.random.key(seed), 4)
    right_side = draw_right_side(jax.random.fold_in(splits[3], 71), 0)
    points = draw_points(jax.random.fold_in(splits[3], 71), 0)
    near_boxes = draw_near_boxes(jax.random.fold_in(splits[3], 71), 0)
    return dict(right_side=right_side, points=points, near_boxes=near_boxes)


NOISE_LEVEL = 0.3
KERNEL_SCALE = 0.15
SUPPORT = 0.5

def wendland(centers, others):
    summed = jnp.zeros((others.shape[0], others.shape[2], centers.shape[1]), jnp.float32)
    for component in range(3):
        difference = others[:, component, :, None] - centers[component][None, None, :]
        summed = summed + difference * difference
    radius = jnp.sqrt(summed) / SUPPORT
    inside = jnp.maximum(1.0 - radius, 0.0)
    return inside * inside * inside * inside * (4.0 * radius + 1.0)

def operate(values, points, near_boxes):
    present = (near_boxes >= 0).astype(jnp.float32)
    clamped = jnp.maximum(near_boxes, 0).astype(jnp.int32)

    def one_box(entry):
        centers, listing, weights = entry
        others = points[listing]
        near_values = values[listing] * weights[:, None, None]
        kernel = wendland(centers, others)
        return jnp.einsum('mrj,mji->ri', near_values, kernel, precision=lax.Precision.HIGHEST, preferred_element_type=jnp.float32)
    products = lax.map(one_box, (points, clamped, present))
    return KERNEL_SCALE * products + NOISE_LEVEL * values

def column_sums(first, second):
    return lax.optimization_barrier(jnp.sum(first * second, axis=(0, 2)))

def reference(right_side, points, near_boxes):
    solution_field = jnp.zeros_like(right_side)
    residual = right_side
    direction = right_side
    norm_now = column_sums(residual, residual)
    for iteration in range(ITERS):
        image_vec = operate(direction, points, near_boxes)
        step_size = norm_now / column_sums(direction, image_vec)
        solution_field = solution_field + step_size[None, :, None] * direction
        residual = residual - step_size[None, :, None] * image_vec
        norm_next = column_sums(residual, residual)
        direction = residual + (norm_next / norm_now)[None, :, None] * direction
        norm_now = norm_next
    return (solution_field, residual)
```

```python
import jax
import jax.numpy as jnp
from jax import lax
from jax.sharding import PartitionSpec as P

GRID_Y = 4


NOISE_LEVEL = 0.3
KERNEL_SCALE = 0.15
SUPPORT = 0.5

AXES = ("leaf", "sub")


def grid_shape():
    count_low = lax.axis_size("sub") // 2
    count_mid = GRID_Y
    total = lax.axis_size("leaf") * lax.axis_size("sub")
    return (total // (count_mid * count_low), count_mid, count_low)


def neighbour_route(shape, dim, step):
    sizes = shape
    route = []
    for dev in range(sizes[0] * sizes[1] * sizes[2]):
        pos = [dev // (sizes[1] * sizes[2]), dev // sizes[2] % sizes[1], dev % sizes[2]]
        pos[dim] += step
        if 0 <= pos[dim] < sizes[dim]:
            source = (pos[0] * sizes[1] + pos[1]) * sizes[2] + pos[2]
            route.append((source, dev))
    return route


HALO_ORDER = (1, 2, 0)


def collect_halo(tile_in, shape):
    current = tile_in
    for dim in HALO_ORDER:
        lower = lax.ppermute(current, AXES, neighbour_route(shape, dim, -1))
        upper = lax.ppermute(current, AXES, neighbour_route(shape, dim, 1))
        current = jnp.concatenate([lower, current, upper], axis=0)
    return current


def wendland(centers, others):
    summed = jnp.zeros((others.shape[0], others.shape[2], centers.shape[1]), jnp.float32)
    for component in range(3):
        difference = others[:, component, :, None] - centers[component][None, None, :]
        summed = summed + difference * difference
    radius = jnp.sqrt(summed) / SUPPORT
    inside = jnp.maximum(1.0 - radius, 0.0)
    return inside * inside * inside * inside * (4.0 * radius + 1.0)


def locate(near_boxes, per_dev, shape):
    count_mid, count_low = shape[1], shape[2]
    own_dev = lax.axis_index(AXES)
    present = (near_boxes >= 0).astype(jnp.float32)
    clamped = jnp.maximum(near_boxes, 0)
    owner_dev = clamped // per_dev
    plane = count_mid * count_low
    step_x = owner_dev // plane - own_dev // plane
    step_y = owner_dev // count_low % count_mid - own_dev // count_low % count_mid
    step_z = owner_dev % count_low - own_dev % count_low
    positions = (((step_x + 1) * 3 + step_z + 1) * 3 + step_y + 1) * per_dev + clamped % per_dev
    positions = jnp.clip(positions, 0, 27 * per_dev - 1)
    return (positions, present)


def column_sums(first, second):
    return jnp.sum(first * second, axis=(0, 2))


def spread(column):
    return column[None, :, None]


def per_device(right_side, points, near_boxes):
    shape = grid_shape()
    per_dev = points.shape[0]
    positions, present = locate(near_boxes, per_dev, shape)
    point_tiles = collect_halo(points, shape)
    others = point_tiles[positions]
    kernel = jax.vmap(wendland)(points, others) * present[:, :, None, None]
    kernel = lax.optimization_barrier(kernel)

    def operate(values):
        gathered = collect_halo(values, shape)
        near_values = gathered[positions]
        products = jnp.einsum(
            "bmrj,bmji->bri",
            near_values,
            kernel,
            precision=lax.Precision.HIGHEST,
            preferred_element_type=jnp.float32,
        )
        return KERNEL_SCALE * products + NOISE_LEVEL * values

    residual0 = right_side
    direction0 = right_side
    image0 = operate(direction0)
    first = lax.psum(
        jnp.stack([column_sums(residual0, residual0), column_sums(direction0, image0)]),
        AXES,
    )
    norm0, curve0 = first[0], first[1]
    step0 = norm0 / curve0
    solution_field = spread(step0) * direction0
    residual1 = residual0 - spread(step0) * image0
    image_res = operate(residual1)
    second = lax.psum(
        jnp.stack(
            [
                column_sums(residual1, residual1),
                column_sums(residual1, image_res),
                column_sums(residual1, image0),
                column_sums(direction0, image_res),
            ]
        ),
        AXES,
    )
    norm1 = second[0]
    ratio = norm1 / norm0
    curve1 = second[1] + ratio * (second[2] + second[3]) + ratio * ratio * curve0
    step1 = norm1 / curve1
    direction1 = residual1 + spread(ratio) * direction0
    image1 = image_res + spread(ratio) * image0
    solution_field = solution_field + spread(step1) * direction1
    residual2 = residual1 - spread(step1) * image1
    return (solution_field, residual2)


def solution(mesh):
    placed = (
        P(AXES, None, None),
        P(AXES, None, None),
        P(AXES, None),
    )
    return jax.shard_map(
        per_device,
        mesh=mesh,
        in_specs=placed,
        out_specs=(P(AXES, None, None), P(AXES, None, None)),
        check_vma=False,
    )
```

```python
import jax
import jax.numpy as jnp
from jax import lax
from jax.sharding import PartitionSpec as P

GRID_Y = 4


NOISE_LEVEL = 0.3
KERNEL_SCALE = 0.15
SUPPORT = 0.5

AXES = ("leaf", "sub")


def grid_shape():
    count_low = lax.axis_size("sub") // 2
    count_mid = GRID_Y
    total = lax.axis_size("leaf") * lax.axis_size("sub")
    return (total // (count_mid * count_low), count_mid, count_low)


def neighbour_route(shape, dim, step):
    sizes = shape
    route = []
    for dev in range(sizes[0] * sizes[1] * sizes[2]):
        pos = [dev // (sizes[1] * sizes[2]), dev // sizes[2] % sizes[1], dev % sizes[2]]
        pos[dim] += step
        if 0 <= pos[dim] < sizes[dim]:
            source = (pos[0] * sizes[1] + pos[1]) * sizes[2] + pos[2]
            route.append((source, dev))
    return route


HALO_ORDER = (1, 2, 0)


def collect_halo(tile_in, shape):
    current = tile_in
    for dim in HALO_ORDER:
        lower = lax.ppermute(current, AXES, neighbour_route(shape, dim, -1))
        upper = lax.ppermute(current, AXES, neighbour_route(shape, dim, 1))
        current = jnp.concatenate([lower, current, upper], axis=0)
    return current


def wendland(centers, others):
    summed = jnp.zeros((others.shape[0], others.shape[2], centers.shape[1]), jnp.float32)
    for component in range(3):
        difference = others[:, component, :, None] - centers[component][None, None, :]
        summed = summed + difference * difference
    radius = jnp.sqrt(summed) / SUPPORT
    inside = jnp.maximum(1.0 - radius, 0.0)
    return inside * inside * inside * inside * (4.0 * radius + 1.0)


def locate(near_boxes, per_dev, shape):
    count_mid, count_low = shape[1], shape[2]
    own_dev = lax.axis_index(AXES)
    present = (near_boxes >= 0).astype(jnp.float32)
    clamped = jnp.maximum(near_boxes, 0)
    owner_dev = clamped // per_dev
    plane = count_mid * count_low
    step_x = owner_dev // plane - own_dev // plane
    step_y = owner_dev // count_low % count_mid - own_dev // count_low % count_mid
    step_z = owner_dev % count_low - own_dev % count_low
    positions = (((step_x + 1) * 3 + step_z + 1) * 3 + step_y + 1) * per_dev + clamped % per_dev
    positions = jnp.clip(positions, 0, 27 * per_dev - 1)
    return (positions, present)


def all_sum(value):
    total = lax.axis_size("leaf") * lax.axis_size("sub")
    bit = 1
    while bit < total:
        value = value + lax.ppermute(value, AXES, [(i, i ^ bit) for i in range(total)])
        bit *= 2
    return value


def column_sums(first, second):
    return jnp.sum(first * second, axis=(0, 2))


def spread(column):
    return column[None, :, None]


def per_device(right_side, points, near_boxes):
    shape = grid_shape()
    per_dev = points.shape[0]
    positions, present = locate(near_boxes, per_dev, shape)
    point_tiles = collect_halo(points, shape)
    others = point_tiles[positions]
    kernel = jax.vmap(wendland)(points, others) * present[:, :, None, None]
    kernel = lax.optimization_barrier(kernel)

    def operate(values):
        gathered = collect_halo(values, shape)
        near_values = gathered[positions]
        products = jnp.einsum(
            "bmrj,bmji->bri",
            near_values,
            kernel,
            precision=lax.Precision.HIGHEST,
            preferred_element_type=jnp.float32,
        )
        return KERNEL_SCALE * products + NOISE_LEVEL * values

    residual0 = right_side
    direction0 = right_side
    image0 = operate(direction0)
    first = all_sum(
        jnp.stack([column_sums(residual0, residual0), column_sums(direction0, image0)])
    )
    norm0, curve0 = first[0], first[1]
    step0 = norm0 / curve0
    solution_field = spread(step0) * direction0
    residual1 = residual0 - spread(step0) * image0
    image_res = operate(residual1)
    second = all_sum(
        jnp.stack(
            [
                column_sums(residual1, residual1),
                column_sums(residual1, image_res),
                column_sums(residual1, image0),
                column_sums(direction0, image_res),
            ]
        )
    )
    norm1 = second[0]
    ratio = norm1 / norm0
    curve1 = second[1] + ratio * (second[2] + second[3]) + ratio * ratio * curve0
    step1 = norm1 / curve1
    direction1 = residual1 + spread(ratio) * direction0
    image1 = image_res + spread(ratio) * image0
    solution_field = solution_field + spread(step1) * direction1
    residual2 = residual1 - spread(step1) * image1
    return (solution_field, residual2)


def solution(mesh):
    placed = (
        P(AXES, None, None),
        P(AXES, None, None),
        P(AXES, None),
    )
    return jax.shard_map(
        per_device,
        mesh=mesh,
        in_specs=placed,
        out_specs=(P(AXES, None, None), P(AXES, None, None)),
        check_vma=False,
    )
```

```python
import jax
import jax.numpy as jnp
from jax import lax
from jax.sharding import PartitionSpec as P

GRID_Y = 4


NOISE_LEVEL = 0.3
KERNEL_SCALE = 0.15
SUPPORT = 0.5

AXES = ("leaf", "sub")


def grid_shape():
    count_low = lax.axis_size("sub") // 2
    count_mid = GRID_Y
    total = lax.axis_size("leaf") * lax.axis_size("sub")
    return (total // (count_mid * count_low), count_mid, count_low)


def neighbour_route(shape, dim, step):
    sizes = shape
    route = []
    for dev in range(sizes[0] * sizes[1] * sizes[2]):
        pos = [dev // (sizes[1] * sizes[2]), dev // sizes[2] % sizes[1], dev % sizes[2]]
        pos[dim] += step
        if 0 <= pos[dim] < sizes[dim]:
            source = (pos[0] * sizes[1] + pos[1]) * sizes[2] + pos[2]
            route.append((source, dev))
    return route


HALO_ORDER = (1, 2, 0)


def collect_halo(tile_in, shape):
    current = tile_in
    for dim in HALO_ORDER:
        lower = lax.ppermute(current, AXES, neighbour_route(shape, dim, -1))
        upper = lax.ppermute(current, AXES, neighbour_route(shape, dim, 1))
        current = jnp.concatenate([lower, current, upper], axis=0)
    return current


def wendland(centers, others):
    summed = jnp.zeros((others.shape[0], others.shape[2], centers.shape[1]), jnp.float32)
    for component in range(3):
        difference = others[:, component, :, None] - centers[component][None, None, :]
        summed = summed + difference * difference
    radius = jnp.sqrt(summed) / SUPPORT
    inside = jnp.maximum(1.0 - radius, 0.0)
    return inside * inside * inside * inside * (4.0 * radius + 1.0)


def locate(near_boxes, per_dev, shape):
    count_mid, count_low = shape[1], shape[2]
    own_dev = lax.axis_index(AXES)
    present = (near_boxes >= 0).astype(jnp.float32)
    clamped = jnp.maximum(near_boxes, 0)
    owner_dev = clamped // per_dev
    plane = count_mid * count_low
    step_x = owner_dev // plane - own_dev // plane
    step_y = owner_dev // count_low % count_mid - own_dev // count_low % count_mid
    step_z = owner_dev % count_low - own_dev % count_low
    positions = (((step_x + 1) * 3 + step_z + 1) * 3 + step_y + 1) * per_dev + clamped % per_dev
    positions = jnp.clip(positions, 0, 27 * per_dev - 1)
    return (positions, present)


def all_sum(value):
    total = lax.axis_size("leaf") * lax.axis_size("sub")
    bit = 1
    while bit < total:
        value = value + lax.ppermute(value, AXES, [(i, i ^ bit) for i in range(total)])
        bit *= 2
    return value


def column_sums(first, second):
    return jnp.sum(first * second, axis=(0, 2))


def spread(column):
    return column[None, :, None]


def per_device(right_side, points, near_boxes):
    shape = grid_shape()
    per_dev = points.shape[0]
    positions, present = locate(near_boxes, per_dev, shape)
    point_tiles = collect_halo(points, shape)
    others = point_tiles[positions]
    kernel = jax.vmap(wendland)(points, others) * present[:, :, None, None]
    kernel = lax.optimization_barrier(kernel)

    def operate(values):
        gathered = collect_halo(values, shape)
        near_values = gathered[positions]
        products = jnp.einsum(
            "bmrj,bmji->bri",
            near_values,
            kernel,
            precision=lax.Precision.HIGHEST,
            preferred_element_type=jnp.float32,
        )
        return KERNEL_SCALE * products + NOISE_LEVEL * values

    residual0 = right_side
    direction0 = right_side
    image0 = operate(direction0)
    first = all_sum(
        jnp.stack([column_sums(residual0, residual0), column_sums(direction0, image0)])
    )
    image_sq = operate(image0)
    norm0, curve0 = first[0], first[1]
    step0 = norm0 / curve0
    solution_field = spread(step0) * direction0
    residual1 = residual0 - spread(step0) * image0
    image_res = image0 - spread(step0) * image_sq
    second = all_sum(
        jnp.stack(
            [
                column_sums(residual1, residual1),
                column_sums(residual1, image_res),
                column_sums(residual1, image0),
                column_sums(direction0, image_res),
            ]
        )
    )
    norm1 = second[0]
    ratio = norm1 / norm0
    curve1 = second[1] + ratio * (second[2] + second[3]) + ratio * ratio * curve0
    step1 = norm1 / curve1
    direction1 = residual1 + spread(ratio) * direction0
    image1 = image_res + spread(ratio) * image0
    solution_field = solution_field + spread(step1) * direction1
    residual2 = residual1 - spread(step1) * image1
    return (solution_field, residual2)


def solution(mesh):
    placed = (
        P(AXES, None, None),
        P(AXES, None, None),
        P(AXES, None),
    )
    return jax.shard_map(
        per_device,
        mesh=mesh,
        in_specs=placed,
        out_specs=(P(AXES, None, None), P(AXES, None, None)),
        check_vma=False,
    )
```

```python
import jax
import jax.numpy as jnp
from jax import lax
from jax.sharding import PartitionSpec as P

GRID_Y = 4


NOISE_LEVEL = 0.3
KERNEL_SCALE = 0.15
SUPPORT = 0.5

AXES = ("leaf", "sub")


def grid_shape():
    count_low = lax.axis_size("sub") // 2
    count_mid = GRID_Y
    total = lax.axis_size("leaf") * lax.axis_size("sub")
    return (total // (count_mid * count_low), count_mid, count_low)


def neighbour_route(shape, dim, step):
    sizes = shape
    route = []
    for dev in range(sizes[0] * sizes[1] * sizes[2]):
        pos = [dev // (sizes[1] * sizes[2]), dev // sizes[2] % sizes[1], dev % sizes[2]]
        pos[dim] += step
        if 0 <= pos[dim] < sizes[dim]:
            source = (pos[0] * sizes[1] + pos[1]) * sizes[2] + pos[2]
            route.append((source, dev))
    return route


HALO_ORDER = (1, 2, 0)


def collect_halo(tile_in, shape):
    current = tile_in
    for dim in HALO_ORDER:
        lower = lax.ppermute(current, AXES, neighbour_route(shape, dim, -1))
        upper = lax.ppermute(current, AXES, neighbour_route(shape, dim, 1))
        current = jnp.concatenate([lower, current, upper], axis=0)
    return current


def wendland(centers, others):
    summed = jnp.zeros((others.shape[0], others.shape[2], centers.shape[1]), jnp.float32)
    for component in range(3):
        difference = others[:, component, :, None] - centers[component][None, None, :]
        summed = summed + difference * difference
    radius = jnp.sqrt(summed) / SUPPORT
    inside = jnp.maximum(1.0 - radius, 0.0)
    return inside * inside * inside * inside * (4.0 * radius + 1.0)


def locate(near_boxes, per_dev, shape):
    count_mid, count_low = shape[1], shape[2]
    own_dev = lax.axis_index(AXES)
    present = (near_boxes >= 0).astype(jnp.float32)
    clamped = jnp.maximum(near_boxes, 0)
    owner_dev = clamped // per_dev
    plane = count_mid * count_low
    step_x = owner_dev // plane - own_dev // plane
    step_y = owner_dev // count_low % count_mid - own_dev // count_low % count_mid
    step_z = owner_dev % count_low - own_dev % count_low
    positions = (((step_x + 1) * 3 + step_z + 1) * 3 + step_y + 1) * per_dev + clamped % per_dev
    positions = jnp.clip(positions, 0, 27 * per_dev - 1)
    return (positions, present)


def all_sum(value):
    total = lax.axis_size("leaf") * lax.axis_size("sub")
    bit = 1
    while bit < total:
        value = value + lax.ppermute(value, AXES, [(i, i ^ bit) for i in range(total)])
        bit *= 2
    return value


def column_sums(first, second):
    return jnp.sum(first * second, axis=(0, 2))


def spread(column):
    return column[None, :, None]


def per_device(right_side, points, near_boxes):
    shape = grid_shape()
    per_dev = points.shape[0]
    positions, present = locate(near_boxes, per_dev, shape)
    point_tiles = collect_halo(points, shape)
    others = point_tiles[positions]
    kernel = jax.vmap(wendland)(points, others) * present[:, :, None, None]
    kernel = lax.optimization_barrier(kernel)

    def operate(values):
        gathered = collect_halo(values, shape)
        near_values = gathered[positions]
        products = jnp.einsum(
            "bmrj,bmji->bri",
            near_values,
            kernel,
            precision=lax.Precision.HIGHEST,
            preferred_element_type=jnp.float32,
        )
        return KERNEL_SCALE * products + NOISE_LEVEL * values

    residual0 = right_side
    direction0 = right_side
    image0 = operate(direction0)
    image_sq = operate(image0)
    moments = all_sum(
        jnp.stack(
            [
                column_sums(residual0, residual0),
                column_sums(residual0, image0),
                column_sums(image0, image0),
                column_sums(residual0, image_sq),
                column_sums(image0, image_sq),
            ]
        )
    )
    norm0, curve0 = moments[0], moments[1]
    step0 = norm0 / curve0
    norm1_est = norm0 - 2.0 * step0 * curve0 + step0 * step0 * moments[2]
    usable = jnp.all(jnp.isfinite(moments))
    usable &= jnp.all(jnp.abs(moments[:3]) > 1e-30)
    usable &= jnp.all(norm1_est >= 0.15 * norm0)

    def from_moments():
        ratio = norm1_est / norm0
        grow = 1.0 + ratio
        curve1 = (
            grow * grow * curve0
            - grow * step0 * (moments[3] + moments[2])
            + step0 * step0 * moments[4]
        )
        step1 = norm1_est / curve1
        total = step0 + step1 * grow
        both = step1 * step0
        solution_field = spread(total) * residual0 - spread(both) * image0
        residual2 = residual0 - spread(total) * image0 + spread(both) * image_sq
        return (solution_field, residual2)

    def from_vectors():
        solution_field = spread(step0) * direction0
        residual1 = residual0 - spread(step0) * image0
        image_res = image0 - spread(step0) * image_sq
        second = all_sum(
            jnp.stack(
                [
                    column_sums(residual1, residual1),
                    column_sums(residual1, image_res),
                    column_sums(residual1, image0),
                    column_sums(direction0, image_res),
                ]
            )
        )
        norm1 = second[0]
        ratio = norm1 / norm0
        curve1 = second[1] + ratio * (second[2] + second[3]) + ratio * ratio * curve0
        step1 = norm1 / curve1
        direction1 = residual1 + spread(ratio) * direction0
        image1 = image_res + spread(ratio) * image0
        solution_field = solution_field + spread(step1) * direction1
        residual2 = residual1 - spread(step1) * image1
        return (solution_field, residual2)

    solution_field, residual2 = lax.cond(usable, from_moments, from_vectors)
    return (solution_field, residual2)


def solution(mesh):
    placed = (
        P(AXES, None, None),
        P(AXES, None, None),
        P(AXES, None),
    )
    return jax.shard_map(
        per_device,
        mesh=mesh,
        in_specs=placed,
        out_specs=(P(AXES, None, None), P(AXES, None, None)),
        check_vma=False,
    )
```

```python
import jax
import jax.numpy as jnp
from jax import lax
from jax.sharding import PartitionSpec as P

GRID_Y = 4


NOISE_LEVEL = 0.3
KERNEL_SCALE = 0.15
SUPPORT = 0.5

AXES = ("leaf", "sub")


def grid_shape():
    count_low = lax.axis_size("sub") // 2
    count_mid = GRID_Y
    total = lax.axis_size("leaf") * lax.axis_size("sub")
    return (total // (count_mid * count_low), count_mid, count_low)


def neighbour_route(shape, dim, step):
    sizes = shape
    route = []
    for dev in range(sizes[0] * sizes[1] * sizes[2]):
        pos = [dev // (sizes[1] * sizes[2]), dev // sizes[2] % sizes[1], dev % sizes[2]]
        pos[dim] += step
        if 0 <= pos[dim] < sizes[dim]:
            source = (pos[0] * sizes[1] + pos[1]) * sizes[2] + pos[2]
            route.append((source, dev))
    return route


HALO_ORDER = (1, 2, 0)


def collect_halo(tile_in, shape):
    current = tile_in
    for dim in HALO_ORDER:
        lower = lax.ppermute(current, AXES, neighbour_route(shape, dim, -1))
        upper = lax.ppermute(current, AXES, neighbour_route(shape, dim, 1))
        current = jnp.concatenate([lower, current, upper], axis=0)
    return current


def wendland(centers, others):
    summed = jnp.zeros((others.shape[0], others.shape[2], centers.shape[1]), jnp.float32)
    for component in range(3):
        difference = others[:, component, :, None] - centers[component][None, None, :]
        summed = summed + difference * difference
    radius = jnp.sqrt(summed) / SUPPORT
    inside = jnp.maximum(1.0 - radius, 0.0)
    return inside * inside * inside * inside * (4.0 * radius + 1.0)


def locate(near_boxes, per_dev, shape):
    count_mid, count_low = shape[1], shape[2]
    own_dev = lax.axis_index(AXES)
    present = (near_boxes >= 0).astype(jnp.float32)
    clamped = jnp.maximum(near_boxes, 0)
    owner_dev = clamped // per_dev
    plane = count_mid * count_low
    step_x = owner_dev // plane - own_dev // plane
    step_y = owner_dev // count_low % count_mid - own_dev // count_low % count_mid
    step_z = owner_dev % count_low - own_dev % count_low
    positions = (((step_x + 1) * 3 + step_z + 1) * 3 + step_y + 1) * per_dev + clamped % per_dev
    positions = jnp.clip(positions, 0, 27 * per_dev - 1)
    return (positions, present)


def all_sum(value):
    total = lax.axis_size("leaf") * lax.axis_size("sub")
    bit = 1
    while bit < total:
        value = value + lax.ppermute(value, AXES, [(i, i ^ bit) for i in range(total)])
        bit *= 2
    return value


def column_sums(first, second):
    return jnp.sum(first * second, axis=(0, 2))


def spread(column):
    return column[None, :, None]


def per_device(right_side, points, near_boxes):
    shape = grid_shape()
    per_dev = points.shape[0]
    positions, present = locate(near_boxes, per_dev, shape)
    joined_tiles = collect_halo(jnp.concatenate([points, right_side], axis=1), shape)
    point_tiles = joined_tiles[:, : points.shape[1]]
    first_tiles = joined_tiles[:, points.shape[1] :]
    others = point_tiles[positions]
    kernel = jax.vmap(wendland)(points, others) * present[:, :, None, None]
    kernel = lax.optimization_barrier(kernel)

    def operate(values, gathered=None):
        if gathered is None:
            gathered = collect_halo(values, shape)
        near_values = gathered[positions]
        products = jnp.einsum(
            "bmrj,bmji->bri",
            near_values,
            kernel,
            precision=lax.Precision.HIGHEST,
            preferred_element_type=jnp.float32,
        )
        return KERNEL_SCALE * products + NOISE_LEVEL * values

    residual0 = right_side
    direction0 = right_side
    image0 = operate(direction0, first_tiles)
    image_sq = operate(image0)
    moments = all_sum(
        jnp.stack(
            [
                column_sums(residual0, residual0),
                column_sums(residual0, image0),
                column_sums(image0, image0),
                column_sums(residual0, image_sq),
                column_sums(image0, image_sq),
            ]
        )
    )
    norm0, curve0 = moments[0], moments[1]
    step0 = norm0 / curve0
    norm1_est = norm0 - 2.0 * step0 * curve0 + step0 * step0 * moments[2]
    usable = jnp.all(jnp.isfinite(moments))
    usable &= jnp.all(jnp.abs(moments[:3]) > 1e-30)
    usable &= jnp.all(norm1_est >= 0.15 * norm0)

    def from_moments():
        ratio = norm1_est / norm0
        grow = 1.0 + ratio
        curve1 = (
            grow * grow * curve0
            - grow * step0 * (moments[3] + moments[2])
            + step0 * step0 * moments[4]
        )
        step1 = norm1_est / curve1
        total = step0 + step1 * grow
        both = step1 * step0
        solution_field = spread(total) * residual0 - spread(both) * image0
        residual2 = residual0 - spread(total) * image0 + spread(both) * image_sq
        return (solution_field, residual2)

    def from_vectors():
        solution_field = spread(step0) * direction0
        residual1 = residual0 - spread(step0) * image0
        image_res = image0 - spread(step0) * image_sq
        second = all_sum(
            jnp.stack(
                [
                    column_sums(residual1, residual1),
                    column_sums(residual1, image_res),
                    column_sums(residual1, image0),
                    column_sums(direction0, image_res),
                ]
            )
        )
        norm1 = second[0]
        ratio = norm1 / norm0
        curve1 = second[1] + ratio * (second[2] + second[3]) + ratio * ratio * curve0
        step1 = norm1 / curve1
        direction1 = residual1 + spread(ratio) * direction0
        image1 = image_res + spread(ratio) * image0
        solution_field = solution_field + spread(step1) * direction1
        residual2 = residual1 - spread(step1) * image1
        return (solution_field, residual2)

    solution_field, residual2 = lax.cond(usable, from_moments, from_vectors)
    return (solution_field, residual2)


def solution(mesh):
    placed = (
        P(AXES, None, None),
        P(AXES, None, None),
        P(AXES, None),
    )
    return jax.shard_map(
        per_device,
        mesh=mesh,
        in_specs=placed,
        out_specs=(P(AXES, None, None), P(AXES, None, None)),
        check_vma=False,
    )
```

```python
import jax
import jax.numpy as jnp
from jax import lax
from jax.sharding import PartitionSpec as P

GRID_Y = 4


NOISE_LEVEL = 0.3
KERNEL_SCALE = 0.15
SUPPORT = 0.5

AXES = ("leaf", "sub")


def grid_shape():
    count_low = lax.axis_size("sub") // 2
    count_mid = GRID_Y
    total = lax.axis_size("leaf") * lax.axis_size("sub")
    return (total // (count_mid * count_low), count_mid, count_low)


def neighbour_route(shape, dim, step):
    sizes = shape
    route = []
    for dev in range(sizes[0] * sizes[1] * sizes[2]):
        pos = [dev // (sizes[1] * sizes[2]), dev // sizes[2] % sizes[1], dev % sizes[2]]
        pos[dim] += step
        if 0 <= pos[dim] < sizes[dim]:
            source = (pos[0] * sizes[1] + pos[1]) * sizes[2] + pos[2]
            route.append((source, dev))
    return route


HALO_ORDER = (1, 2, 0)


def collect_halo(tile_in, shape):
    current = tile_in
    for dim in HALO_ORDER:
        lower = lax.ppermute(current, AXES, neighbour_route(shape, dim, -1))
        upper = lax.ppermute(current, AXES, neighbour_route(shape, dim, 1))
        current = jnp.concatenate([lower, current, upper], axis=0)
    return current


def wendland(centers, others):
    summed = jnp.zeros((others.shape[0], others.shape[2], centers.shape[1]), jnp.float32)
    for component in range(3):
        difference = others[:, component, :, None] - centers[component][None, None, :]
        summed = summed + difference * difference
    radius = jnp.sqrt(summed) / SUPPORT
    inside = jnp.maximum(1.0 - radius, 0.0)
    return inside * inside * inside * inside * (4.0 * radius + 1.0)


def locate(near_boxes, per_dev, shape):
    count_mid, count_low = shape[1], shape[2]
    own_dev = lax.axis_index(AXES)
    present = (near_boxes >= 0).astype(jnp.float32)
    clamped = jnp.maximum(near_boxes, 0)
    owner_dev = clamped // per_dev
    plane = count_mid * count_low
    step_x = owner_dev // plane - own_dev // plane
    step_y = owner_dev // count_low % count_mid - own_dev // count_low % count_mid
    step_z = owner_dev % count_low - own_dev % count_low
    positions = (((step_x + 1) * 3 + step_z + 1) * 3 + step_y + 1) * per_dev + clamped % per_dev
    positions = jnp.clip(positions, 0, 27 * per_dev - 1)
    return (positions, present)


def all_sum(value):
    for axis in ("sub", "leaf"):
        size = lax.axis_size(axis)
        copies = jnp.broadcast_to(value[None], (size,) + value.shape)
        value = jnp.sum(lax.all_to_all(copies, axis, 0, 0, tiled=False), axis=0)
    return value


def column_sums(first, second):
    return jnp.sum(first * second, axis=(0, 2))


def spread(column):
    return column[None, :, None]


def per_device(right_side, points, near_boxes):
    shape = grid_shape()
    per_dev = points.shape[0]
    positions, present = locate(near_boxes, per_dev, shape)
    point_tiles = collect_halo(points, shape)
    others = point_tiles[positions]
    kernel = jax.vmap(wendland)(points, others) * present[:, :, None, None]
    kernel = lax.optimization_barrier(kernel)

    def operate(values):
        gathered = collect_halo(values, shape)
        near_values = gathered[positions]
        products = jnp.einsum(
            "bmrj,bmji->bri",
            near_values,
            kernel,
            precision=lax.Precision.HIGHEST,
            preferred_element_type=jnp.float32,
        )
        return KERNEL_SCALE * products + NOISE_LEVEL * values

    residual0 = right_side
    direction0 = right_side
    image0 = operate(direction0)
    image_sq = operate(image0)
    moments = all_sum(
        jnp.stack(
            [
                column_sums(residual0, residual0),
                column_sums(residual0, image0),
                column_sums(image0, image0),
                column_sums(residual0, image_sq),
                column_sums(image0, image_sq),
            ]
        )
    )
    norm0, curve0 = moments[0], moments[1]
    step0 = norm0 / curve0
    norm1_est = norm0 - 2.0 * step0 * curve0 + step0 * step0 * moments[2]
    usable = jnp.all(jnp.isfinite(moments))
    usable &= jnp.all(jnp.abs(moments[:3]) > 1e-30)
    usable &= jnp.all(norm1_est >= 0.15 * norm0)

    def from_moments():
        ratio = norm1_est / norm0
        grow = 1.0 + ratio
        curve1 = (
            grow * grow * curve0
            - grow * step0 * (moments[3] + moments[2])
            + step0 * step0 * moments[4]
        )
        step1 = norm1_est / curve1
        total = step0 + step1 * grow
        both = step1 * step0
        solution_field = spread(total) * residual0 - spread(both) * image0
        residual2 = residual0 - spread(total) * image0 + spread(both) * image_sq
        return (solution_field, residual2)

    def from_vectors():
        solution_field = spread(step0) * direction0
        residual1 = residual0 - spread(step0) * image0
        image_res = image0 - spread(step0) * image_sq
        second = all_sum(
            jnp.stack(
                [
                    column_sums(residual1, residual1),
                    column_sums(residual1, image_res),
                    column_sums(residual1, image0),
                    column_sums(direction0, image_res),
                ]
            )
        )
        norm1 = second[0]
        ratio = norm1 / norm0
        curve1 = second[1] + ratio * (second[2] + second[3]) + ratio * ratio * curve0
        step1 = norm1 / curve1
        direction1 = residual1 + spread(ratio) * direction0
        image1 = image_res + spread(ratio) * image0
        solution_field = solution_field + spread(step1) * direction1
        residual2 = residual1 - spread(step1) * image1
        return (solution_field, residual2)

    solution_field, residual2 = lax.cond(usable, from_moments, from_vectors)
    return (solution_field, residual2)


def solution(mesh):
    placed = (
        P(AXES, None, None),
        P(AXES, None, None),
        P(AXES, None),
    )
    return jax.shard_map(
        per_device,
        mesh=mesh,
        in_specs=placed,
        out_specs=(P(AXES, None, None), P(AXES, None, None)),
        check_vma=False,
    )
```

```python
import jax
import jax.numpy as jnp
from jax import lax
from jax.sharding import PartitionSpec as P

GRID_Y = 4


NOISE_LEVEL = 0.3
KERNEL_SCALE = 0.15
SUPPORT = 0.5

AXES = ("leaf", "sub")


def grid_shape():
    count_low = lax.axis_size("sub") // 2
    count_mid = GRID_Y
    total = lax.axis_size("leaf") * lax.axis_size("sub")
    return (total // (count_mid * count_low), count_mid, count_low)


def neighbour_route(shape, dim, step):
    sizes = shape
    route = []
    for dev in range(sizes[0] * sizes[1] * sizes[2]):
        pos = [dev // (sizes[1] * sizes[2]), dev // sizes[2] % sizes[1], dev % sizes[2]]
        pos[dim] += step
        if 0 <= pos[dim] < sizes[dim]:
            source = (pos[0] * sizes[1] + pos[1]) * sizes[2] + pos[2]
            route.append((source, dev))
    return route


HALO_ORDER = (1, 2, 0)


def collect_halo(tile_in, shape):
    current = tile_in
    for dim in HALO_ORDER:
        lower = lax.ppermute(current, AXES, neighbour_route(shape, dim, -1))
        upper = lax.ppermute(current, AXES, neighbour_route(shape, dim, 1))
        current = jnp.concatenate([lower, current, upper], axis=0)
    return current


def wendland(centers, others):
    summed = jnp.zeros((others.shape[0], others.shape[2], centers.shape[1]), jnp.float32)
    for component in range(3):
        difference = others[:, component, :, None] - centers[component][None, None, :]
        summed = summed + difference * difference
    radius = jnp.sqrt(summed) / SUPPORT
    inside = jnp.maximum(1.0 - radius, 0.0)
    return inside * inside * inside * inside * (4.0 * radius + 1.0)


def locate(near_boxes, per_dev, shape):
    count_mid, count_low = shape[1], shape[2]
    own_dev = lax.axis_index(AXES)
    present = (near_boxes >= 0).astype(jnp.float32)
    clamped = jnp.maximum(near_boxes, 0)
    owner_dev = clamped // per_dev
    plane = count_mid * count_low
    step_x = owner_dev // plane - own_dev // plane
    step_y = owner_dev // count_low % count_mid - own_dev // count_low % count_mid
    step_z = owner_dev % count_low - own_dev % count_low
    positions = (((step_x + 1) * 3 + step_z + 1) * 3 + step_y + 1) * per_dev + clamped % per_dev
    positions = jnp.clip(positions, 0, 27 * per_dev - 1)
    return (positions, present)


def all_sum(value):
    for axis in ("sub", "leaf"):
        size = lax.axis_size(axis)
        copies = jnp.broadcast_to(value[None], (size,) + value.shape)
        value = jnp.sum(lax.all_to_all(copies, axis, 0, 0, tiled=False), axis=0)
    return value


def column_sums(first, second):
    return jnp.sum(first * second, axis=(0, 2))


def spread(column):
    return column[None, :, None]


def per_device(right_side, points, near_boxes):
    shape = grid_shape()
    per_dev = points.shape[0]
    positions, present = locate(near_boxes, per_dev, shape)
    point_tiles = collect_halo(points, shape)
    others = point_tiles[positions]
    kernel = jax.vmap(wendland)(points, others) * present[:, :, None, None]
    kernel = lax.optimization_barrier(kernel)

    def operate(values):
        gathered = collect_halo(values, shape)
        near_values = gathered[positions]
        products = jnp.einsum(
            "bmrj,bmji->bri",
            near_values,
            kernel,
            precision=lax.Precision.HIGH,
            preferred_element_type=jnp.float32,
        )
        return KERNEL_SCALE * products + NOISE_LEVEL * values

    residual0 = right_side
    direction0 = right_side
    image0 = operate(direction0)
    image_sq = operate(image0)
    moments = all_sum(
        jnp.stack(
            [
                column_sums(residual0, residual0),
                column_sums(residual0, image0),
                column_sums(image0, image0),
                column_sums(residual0, image_sq),
                column_sums(image0, image_sq),
            ]
        )
    )
    norm0, curve0 = moments[0], moments[1]
    step0 = norm0 / curve0
    norm1_est = norm0 - 2.0 * step0 * curve0 + step0 * step0 * moments[2]
    usable = jnp.all(jnp.isfinite(moments))
    usable &= jnp.all(jnp.abs(moments[:3]) > 1e-30)
    usable &= jnp.all(norm1_est >= 0.15 * norm0)

    def from_moments():
        ratio = norm1_est / norm0
        grow = 1.0 + ratio
        curve1 = (
            grow * grow * curve0
            - grow * step0 * (moments[3] + moments[2])
            + step0 * step0 * moments[4]
        )
        step1 = norm1_est / curve1
        total = step0 + step1 * grow
        both = step1 * step0
        solution_field = spread(total) * residual0 - spread(both) * image0
        residual2 = residual0 - spread(total) * image0 + spread(both) * image_sq
        return (solution_field, residual2)

    def from_vectors():
        solution_field = spread(step0) * direction0
        residual1 = residual0 - spread(step0) * image0
        image_res = image0 - spread(step0) * image_sq
        second = all_sum(
            jnp.stack(
                [
                    column_sums(residual1, residual1),
                    column_sums(residual1, image_res),
                    column_sums(residual1, image0),
                    column_sums(direction0, image_res),
                ]
            )
        )
        norm1 = second[0]
        ratio = norm1 / norm0
        curve1 = second[1] + ratio * (second[2] + second[3]) + ratio * ratio * curve0
        step1 = norm1 / curve1
        direction1 = residual1 + spread(ratio) * direction0
        image1 = image_res + spread(ratio) * image0
        solution_field = solution_field + spread(step1) * direction1
        residual2 = residual1 - spread(step1) * image1
        return (solution_field, residual2)

    solution_field, residual2 = lax.cond(usable, from_moments, from_vectors)
    return (solution_field, residual2)


def solution(mesh):
    placed = (
        P(AXES, None, None),
        P(AXES, None, None),
        P(AXES, None),
    )
    return jax.shard_map(
        per_device,
        mesh=mesh,
        in_specs=placed,
        out_specs=(P(AXES, None, None), P(AXES, None, None)),
        check_vma=False,
    )
```

```python
import jax
import jax.numpy as jnp
from jax import lax
from jax.sharding import PartitionSpec as P

GRID_Y = 4


NOISE_LEVEL = 0.3
KERNEL_SCALE = 0.15
SUPPORT = 0.5

AXES = ("leaf", "sub")


def grid_shape():
    count_low = lax.axis_size("sub") // 2
    count_mid = GRID_Y
    total = lax.axis_size("leaf") * lax.axis_size("sub")
    return (total // (count_mid * count_low), count_mid, count_low)


def neighbour_route(shape, dim, step):
    sizes = shape
    route = []
    for dev in range(sizes[0] * sizes[1] * sizes[2]):
        pos = [dev // (sizes[1] * sizes[2]), dev // sizes[2] % sizes[1], dev % sizes[2]]
        pos[dim] += step
        if 0 <= pos[dim] < sizes[dim]:
            source = (pos[0] * sizes[1] + pos[1]) * sizes[2] + pos[2]
            route.append((source, dev))
    return route


HALO_ORDER = (2, 1, 0)


def collect_halo(tile_in, shape):
    current = tile_in
    for dim in HALO_ORDER:
        lower = lax.ppermute(current, AXES, neighbour_route(shape, dim, -1))
        upper = lax.ppermute(current, AXES, neighbour_route(shape, dim, 1))
        current = jnp.concatenate([lower, current, upper], axis=0)
    return current


def wendland(centers, others):
    summed = jnp.zeros((others.shape[0], others.shape[2], centers.shape[1]), jnp.float32)
    for component in range(3):
        difference = others[:, component, :, None] - centers[component][None, None, :]
        summed = summed + difference * difference
    radius = jnp.sqrt(summed) / SUPPORT
    inside = jnp.maximum(1.0 - radius, 0.0)
    return inside * inside * inside * inside * (4.0 * radius + 1.0)


def locate(near_boxes, per_dev, shape):
    count_mid, count_low = shape[1], shape[2]
    own_dev = lax.axis_index(AXES)
    present = (near_boxes >= 0).astype(jnp.float32)
    clamped = jnp.maximum(near_boxes, 0)
    owner_dev = clamped // per_dev
    plane = count_mid * count_low
    step_x = owner_dev // plane - own_dev // plane
    step_y = owner_dev // count_low % count_mid - own_dev // count_low % count_mid
    step_z = owner_dev % count_low - own_dev % count_low
    positions = (((step_x + 1) * 3 + step_y + 1) * 3 + step_z + 1) * per_dev + clamped % per_dev
    positions = jnp.clip(positions, 0, 27 * per_dev - 1)
    return (positions, present)


def all_sum(value):
    for axis in ("sub", "leaf"):
        size = lax.axis_size(axis)
        copies = jnp.broadcast_to(value[None], (size,) + value.shape)
        value = jnp.sum(lax.all_to_all(copies, axis, 0, 0, tiled=False), axis=0)
    return value


def column_sums(first, second):
    return jnp.sum(first * second, axis=(0, 2))


def spread(column):
    return column[None, :, None]


def per_device(right_side, points, near_boxes):
    shape = grid_shape()
    per_dev = points.shape[0]
    positions, present = locate(near_boxes, per_dev, shape)
    point_tiles = collect_halo(points, shape)
    others = point_tiles[positions]
    kernel = jax.vmap(wendland)(points, others) * present[:, :, None, None]
    kernel = lax.optimization_barrier(kernel)

    def operate(values):
        gathered = collect_halo(values, shape)
        near_values = gathered[positions]
        products = jnp.einsum(
            "bmrj,bmji->bri",
            near_values,
            kernel,
            precision=lax.Precision.HIGH,
            preferred_element_type=jnp.float32,
        )
        return KERNEL_SCALE * products + NOISE_LEVEL * values

    residual0 = right_side
    direction0 = right_side
    image0 = operate(direction0)
    image_sq = operate(image0)
    moments = all_sum(
        jnp.stack(
            [
                column_sums(residual0, residual0),
                column_sums(residual0, image0),
                column_sums(image0, image0),
                column_sums(residual0, image_sq),
                column_sums(image0, image_sq),
            ]
        )
    )
    norm0, curve0 = moments[0], moments[1]
    step0 = norm0 / curve0
    norm1_est = norm0 - 2.0 * step0 * curve0 + step0 * step0 * moments[2]
    usable = jnp.all(jnp.isfinite(moments))
    usable &= jnp.all(jnp.abs(moments[:3]) > 1e-30)
    usable &= jnp.all(norm1_est >= 0.15 * norm0)

    def from_moments():
        ratio = norm1_est / norm0
        grow = 1.0 + ratio
        curve1 = (
            grow * grow * curve0
            - grow * step0 * (moments[3] + moments[2])
            + step0 * step0 * moments[4]
        )
        step1 = norm1_est / curve1
        total = step0 + step1 * grow
        both = step1 * step0
        solution_field = spread(total) * residual0 - spread(both) * image0
        residual2 = residual0 - spread(total) * image0 + spread(both) * image_sq
        return (solution_field, residual2)

    def from_vectors():
        solution_field = spread(step0) * direction0
        residual1 = residual0 - spread(step0) * image0
        image_res = image0 - spread(step0) * image_sq
        second = all_sum(
            jnp.stack(
                [
                    column_sums(residual1, residual1),
                    column_sums(residual1, image_res),
                    column_sums(residual1, image0),
                    column_sums(direction0, image_res),
                ]
            )
        )
        norm1 = second[0]
        ratio = norm1 / norm0
        curve1 = second[1] + ratio * (second[2] + second[3]) + ratio * ratio * curve0
        step1 = norm1 / curve1
        direction1 = residual1 + spread(ratio) * direction0
        image1 = image_res + spread(ratio) * image0
        solution_field = solution_field + spread(step1) * direction1
        residual2 = residual1 - spread(step1) * image1
        return (solution_field, residual2)

    solution_field, residual2 = lax.cond(usable, from_moments, from_vectors)
    return (solution_field, residual2)


def solution(mesh):
    placed = (
        P(AXES, None, None),
        P(AXES, None, None),
        P(AXES, None),
    )
    return jax.shard_map(
        per_device,
        mesh=mesh,
        in_specs=placed,
        out_specs=(P(AXES, None, None), P(AXES, None, None)),
        check_vma=False,
    )
```
